512 devices in a mesh: section: 32 (over z, x), et: 16 (over y, core).
Axes of the slice: x: 4, y: 8, z: 8, core: 2. Of those that a mesh axis runs over, the one named last changes fastest.
Arguments:
- x_fwd: bfloat16 [32, 256, 3072], P('section', 'et'), may hold values from -6 to 6
- act_fwd: bfloat16 [32, 256, 8192], P('section', None, 'et'), may hold values from -6 to 6
- ids_fwd: int32 [32, 256, 2], P('section'), may hold values from 0 to 7, as said below
- x_bwd: bfloat16 [32, 256, 3072], P('section', 'et'), may hold values from -6 to 6
- act_bwd: bfloat16 [32, 256, 8192], P('section', None, 'et'), may hold values from -6 to 6
- ids_bwd: int32 [32, 256, 2], P('section'), may hold values from 0 to 7, as said below
- grad_out: bfloat16 [32, 256, 3072], P('section', 'et'), may hold values from -6 to 6
- gain: bfloat16 [32, 3072], P('section'), may hold values from 0.099609375 to 1.8984375
- w_router: bfloat16 [32, 3072, 8], P('section'), may hold values from -0.21875 to 0.21875
- w_down: bfloat16 [32, 8192, 3072], P('section', 'et'), may hold values from -0.0625 to 0.0625
Outputs:
- fwd_in: bfloat16 [32, 256, 3072], P('section', 'et')
- incoming_gradient: bfloat16 [32, 256, 3072], P('section', 'et')
- dact: bfloat16 [32, 256, 8192], P('section', None, 'et')
The draws below stay inside these ranges and needn't reach their ends.
Inputs may be any that keep to these rules, and one draw needn't show every extreme that they name: `ids_fwd`: each token names 2 different experts; in each section's micro-batch exactly 128 tokens name expert 0. `ids_bwd`: each token names 2 different experts; in each section's micro-batch exactly 128 tokens name expert 0.
All inputs are finite; a program needn't handle non-finite values.
Results may differ from the reference program's by a relative error of at most 0.014.
Values may be sent and summed in bfloat16 or wider, within the bound.
No kernel may reach another device: no remote copies, remote signals or barrier semaphores. Data moves between devices by JAX's collectives and lax.ppermute only.
A program may use at most 64 MiB of HBM per device.

```python
import jax
import jax.numpy as jnp
from jax import lax

D = 3072
FF_DEV = 512
EXPERT_COUNT = 8
TOK = 256
CAP = 128
FF = 8192
SECTIONS = 32
N_ET = 16


def route_ids(key):
    keys = jax.random.split(jax.random.fold_in(key, 1), SECTIONS)
    ranks = jax.vmap(lambda single: jax.random.permutation(single, TOK))(keys).astype(jnp.int32)
    routed = ranks < CAP
    first_other = jax.random.randint(jax.random.fold_in(key, 2), (SECTIONS, TOK), 1, 8).astype(jnp.int32)
    offset = jax.random.randint(jax.random.fold_in(key, 3), (SECTIONS, TOK), 1, 7).astype(jnp.int32)
    second_other = 1 + (first_other - 1 + offset) % 7
    flip = jax.random.randint(jax.random.fold_in(key, 4), (SECTIONS, TOK), 0, 2).astype(jnp.int32)
    lead = jnp.where(routed, 0, first_other)
    trail = jnp.where(routed, first_other, second_other)
    column_a = jnp.where(flip == 1, trail, lead)
    column_b = jnp.where(flip == 1, lead, trail)
    return jnp.stack([column_a, column_b], axis=-1).astype(jnp.int32)


def draw_ids_fwd(key, part):
    return route_ids(jax.random.fold_in(key, 11))


def draw_ids_bwd(key, part):
    return route_ids(jax.random.fold_in(key, 23))


def steps_of(stream_key, dims, cuts, smallest, largest):
    def one(dim, parts):
        draws = jax.random.uniform(jax.random.fold_in(jax.random.fold_in(stream_key, 6), dim), (parts,), jnp.float32, smallest / len(cuts), largest / len(cuts))
        return jnp.repeat(jnp.exp(draws), dims[dim] // parts).reshape((-1,) + (1,) * (len(dims) - dim - 1))

    level = one(*cuts[0])
    for cut in cuts[1:]:
        level = level * one(*cut)
    return level


def normal_values(key, extent, width, most, cuts=(), kind=jnp.bfloat16):
    result = jax.random.normal(key, extent, jnp.float32) * width
    if len(cuts) > 0:
        result = steps_of(key, extent, cuts, -0.22, 0.18) * result
    return jnp.clip(result, min=-most, max=most).astype(kind)


def setup_inputs(seed: int = 0) -> dict:
    streams_of = jax.random.split(jax.random.key(seed), 11)
    x_fwd = normal_values(streams_of[0], (SECTIONS, TOK, D), 1.0, 6.0, ((0, 32), (1, 16)))
    act_fwd = normal_values(streams_of[1], (SECTIONS, TOK, FF), 1.0, 6.0, ((0, 32), (2, 16)))
    ids_fwd = draw_ids_fwd(jax.random.fold_in(streams_of[10], 71), 0)
    x_bwd = normal_values(streams_of[3], (SECTIONS, TOK, D), 1.0, 6.0, ((0, 32), (1, 16)))
    act_bwd = normal_values(streams_of[4], (SECTIONS, TOK, FF), 1.0, 6.0, ((0, 32), (2, 16)))
    ids_bwd = draw_ids_bwd(jax.random.fold_in(streams_of[10], 71), 0)
    grad_out = normal_values(streams_of[6], (SECTIONS, TOK, D), 1.0, 6.0, ((0, 32), (1, 16)))
    gain = jnp.clip(1.0 + 0.18 * jax.random.normal(streams_of[7], (SECTIONS, D), jnp.float32), 0.099609375, 1.8984375).astype(jnp.bfloat16)
    w_router = normal_values(streams_of[8], (SECTIONS, D, EXPERT_COUNT), (D // 4) ** -0.5, 0.21875, ((0, 32),))
    w_down = normal_values(streams_of[9], (SECTIONS, FF, D), FF ** -0.5, 0.0625, ((0, 32), (1, 16)))
    return {"x_fwd": x_fwd, "act_fwd": act_fwd, "ids_fwd": ids_fwd, "x_bwd": x_bwd, "act_bwd": act_bwd, "ids_bwd": ids_bwd, "grad_out": grad_out, "gain": gain, "w_router": w_router, "w_down": w_down}


def norm_logits(inputs, gain, w_router):
    wide = inputs.astype(jnp.float32)
    inverse = lax.rsqrt(lax.optimization_barrier(jnp.mean(wide * wide, axis=-1, keepdims=True)) + 1e-05)
    normed = (wide * inverse * gain.astype(jnp.float32)).astype(jnp.bfloat16)
    logits = jnp.dot(normed, w_router, preferred_element_type=jnp.float32).astype(jnp.bfloat16)
    return (wide, inverse, logits)

def routing(logits, chosen):
    route = lax.optimization_barrier(jnp.sum((chosen == 0).astype(jnp.float32), axis=1))
    partner = jnp.minimum(lax.optimization_barrier(jnp.sum(chosen, axis=1)), EXPERT_COUNT - 1).astype(jnp.int32)
    labels = jnp.arange(EXPERT_COUNT, dtype=jnp.int32)
    onehot = (partner[:, None] == labels[None, :]).astype(jnp.float32)
    wide_logits = logits.astype(jnp.float32)
    sigma = jax.nn.sigmoid(wide_logits[:, 0] - lax.optimization_barrier(jnp.sum(wide_logits * onehot, axis=1)))
    return (route, onehot, sigma, route * sigma)

def section_pass(inputs):
    x_fwd, act_fwd, ids_fwd, x_bwd, act_bwd, ids_bwd, grad_out, gain, w_router, w_down = inputs
    wide, inverse, logits = norm_logits(x_fwd, gain, w_router)
    route, onehot, sigma, coef = routing(logits, ids_fwd)
    act_groups = act_fwd.reshape(TOK, N_ET, FF_DEV).transpose(1, 0, 2)
    down_groups = w_down.reshape(N_ET, FF_DEV, D)

    def add_group(total, pair):
        acts, weights = pair
        part = jnp.dot(acts, weights, preferred_element_type=jnp.float32) * coef[:, None]
        rounded = lax.optimization_barrier(part.astype(jnp.bfloat16)).astype(jnp.float32)
        return (total + rounded, None)
    total, unused = lax.scan(add_group, jnp.zeros((TOK, D), jnp.float32), (act_groups, down_groups))
    forward_out = (wide + total).astype(jnp.bfloat16)
    backward_wide_rows, backward_inverse_norm, logits_b = norm_logits(x_bwd, gain, w_router)
    route_b, onehot_b, sigma_b, backward_coefficient = routing(logits_b, ids_bwd)
    back_up = jnp.dot(grad_out, w_down.T, preferred_element_type=jnp.float32)
    dact = (backward_coefficient[:, None] * back_up).astype(jnp.bfloat16)
    dprob = lax.optimization_barrier(jnp.sum(act_bwd.astype(jnp.float32) * back_up, axis=1))
    slope = route_b * dprob * sigma_b * (1.0 - sigma_b)
    router_wide = w_router.astype(jnp.float32)
    spread = router_wide[:, 0][None, :] - jnp.dot(onehot_b, router_wide.T, precision=lax.Precision.HIGHEST)
    dnormed = slope[:, None] * spread
    scaled_rows = dnormed * gain.astype(jnp.float32)
    normalized_input = backward_wide_rows * backward_inverse_norm
    norm_input_gradient = backward_inverse_norm * (scaled_rows - normalized_input * lax.optimization_barrier(jnp.mean(scaled_rows * normalized_input, axis=-1, keepdims=True)))
    backward_out = (grad_out.astype(jnp.float32) + norm_input_gradient).astype(jnp.bfloat16)
    return (forward_out, backward_out, dact)

def reference(x_fwd, act_fwd, ids_fwd, x_bwd, act_bwd, ids_bwd, grad_out, gain, w_router, w_down):
    outputs, grads, dact = lax.map(section_pass, (x_fwd, act_fwd, ids_fwd, x_bwd, act_bwd, ids_bwd, grad_out, gain, w_router, w_down))
    fwd_in = jnp.concatenate([jnp.zeros_like(outputs[:1]), outputs[:-1]], axis=0)
    incoming_gradient = jnp.concatenate([grads[1:], jnp.zeros_like(grads[:1])], axis=0)
    return (fwd_in, incoming_gradient, dact)
```

```python
import jax
import jax.numpy as jnp
from jax import lax
from jax.sharding import PartitionSpec as P


def from_behind(value, axis, steps):
    count = lax.axis_size(axis)
    first, last = (max(0, -steps), min(count, count - steps))
    return lax.ppermute(value, axis, [(source, source + steps) for source in range(first, last)])


def norm_logits(inputs, gain, w_router):
    wide = inputs.astype(jnp.float32)
    inverse = lax.rsqrt(jnp.mean(wide * wide, axis=-1, keepdims=True) + 1e-05)
    normed = (wide * inverse * gain.astype(jnp.float32)).astype(jnp.bfloat16)
    logits = jnp.dot(normed, w_router, preferred_element_type=jnp.float32).astype(jnp.bfloat16)
    return (wide, inverse, logits)


def routing(logits, chosen, experts):
    route = jnp.sum((chosen == 0).astype(jnp.float32), axis=1)
    partner = jnp.minimum(jnp.sum(chosen, axis=1), experts - 1)
    labels = jnp.arange(experts, dtype=jnp.int32)
    onehot = (partner[:, None] == labels[None, :]).astype(jnp.float32)
    wide_logits = logits.astype(jnp.float32)
    sigma = jax.nn.sigmoid(wide_logits[:, 0] - jnp.sum(wide_logits * onehot, axis=1))
    return (route, onehot, sigma, route * sigma)


def shards(x_fwd, act_fwd, ids_fwd, x_bwd, act_bwd, ids_bwd, grad_out, gain, w_router, w_down):
    x_fwd, act_fwd, ids_fwd, x_bwd, act_bwd = (x_fwd[0], act_fwd[0], ids_fwd[0], x_bwd[0], act_bwd[0])
    ids_bwd, grad_out, gain, w_router, w_down = (ids_bwd[0], grad_out[0], gain[0], w_router[0], w_down[0])
    experts = w_router.shape[1]
    width = x_fwd.shape[1]
    own_rows = x_fwd.shape[0]
    groups = lax.axis_size("et")
    first_row = lax.axis_index("et") * own_rows
    pad = 128

    wide_f, inverse_f, logit_f = norm_logits(x_fwd, gain, w_router)
    backward_wide_rows, backward_inverse_norm, logit_b = norm_logits(x_bwd, gain, w_router)

    packed = jnp.concatenate(
        [grad_out, jnp.pad(logit_b, ((0, 0), (0, pad - experts)))], axis=1
    )
    tiled = jnp.broadcast_to(packed[None], (groups,) + packed.shape).reshape(groups * own_rows, -1)
    full = lax.all_to_all(tiled, "et", 0, 0, tiled=True)
    full_g = full[:, :width]
    full_b = full[:, width : width + experts]

    route_b, onehot_b, sigma_b, coef_b = routing(full_b, ids_bwd, experts)
    back_up = lax.dot_general(
        full_g, w_down, (((1,), (1,)), ((), ())), preferred_element_type=jnp.float32
    )
    dact = (coef_b[:, None] * back_up).astype(jnp.bfloat16)
    dprob_part = jnp.sum(act_bwd.astype(jnp.float32) * back_up, axis=1)
    dprob_hi = dprob_part.astype(jnp.bfloat16)
    dprob_lo = (dprob_part - dprob_hi.astype(jnp.float32)).astype(jnp.bfloat16)

    z_fwd = jnp.dot(act_fwd, w_down, preferred_element_type=jnp.float32).astype(jnp.bfloat16)
    extra = jnp.zeros((z_fwd.shape[0], pad), jnp.bfloat16)
    extra = extra.at[:, 0].set(dprob_hi).at[:, 1].set(dprob_lo)
    sent = jnp.concatenate([z_fwd, extra], axis=1)
    got = lax.all_to_all(sent, "et", 0, 0, tiled=True).reshape(groups, own_rows, -1)
    got = got.astype(jnp.float32)
    z_sum = jnp.sum(got[:, :, :width], axis=0)
    dprob_mine = jnp.sum(got[:, :, width] + got[:, :, width + 1], axis=0)

    ids_f_own = lax.dynamic_slice_in_dim(ids_fwd, first_row, own_rows, 0)
    _, _, _, coef_f = routing(logit_f, ids_f_own, experts)
    layer_out = (wide_f + coef_f[:, None] * z_sum).astype(jnp.bfloat16)

    ids_b_own = lax.dynamic_slice_in_dim(ids_bwd, first_row, own_rows, 0)
    route_mine, onehot_mine, sigma_mine, _ = routing(logit_b, ids_b_own, experts)
    slope = route_mine * dprob_mine * sigma_mine * (1.0 - sigma_mine)
    router_wide = w_router.astype(jnp.float32)
    spread = router_wide[:, 0][None, :] - jnp.dot(
        onehot_mine, router_wide.T, precision=lax.Precision.HIGHEST
    )
    dnormed = slope[:, None] * spread
    scaled_rows = dnormed * gain.astype(jnp.float32)
    normalized_input = backward_wide_rows * backward_inverse_norm
    norm_input_gradient = backward_inverse_norm * (
        scaled_rows
        - normalized_input * jnp.mean(scaled_rows * normalized_input, axis=-1, keepdims=True)
    )
    input_grad = (grad_out.astype(jnp.float32) + norm_input_gradient).astype(jnp.bfloat16)
    fwd_in = from_behind(layer_out, "section", 1)
    incoming_gradient = from_behind(input_grad, "section", -1)
    return (fwd_in[None], incoming_gradient[None], dact[None])


def solution(mesh):
    placed = (
        P("section", "et", None),
        P("section", None, "et"),
        P("section", None, None),
        P("section", "et", None),
        P("section", None, "et"),
        P("section", None, None),
        P("section", "et", None),
        P("section", None),
        P("section", None, None),
        P("section", "et", None),
    )
    return jax.shard_map(
        shards,
        mesh=mesh,
        in_specs=placed,
        out_specs=(P("section", "et", None), P("section", "et", None), P("section", None, "et")),
        check_vma=False,
    )
```

```python
import jax
import jax.numpy as jnp
from jax import lax
from jax.sharding import PartitionSpec as P


def from_behind(value, axis, steps):
    count = lax.axis_size(axis)
    first, last = (max(0, -steps), min(count, count - steps))
    return lax.ppermute(value, axis, [(source, source + steps) for source in range(first, last)])


def norm_logits(inputs, gain, w_router):
    wide = inputs.astype(jnp.float32)
    inverse = lax.rsqrt(jnp.mean(wide * wide, axis=-1, keepdims=True) + 1e-05)
    normed = (wide * inverse * gain.astype(jnp.float32)).astype(jnp.bfloat16)
    logits = jnp.dot(normed, w_router, preferred_element_type=jnp.float32).astype(jnp.bfloat16)
    return (wide, inverse, logits)


def routing(logits, chosen, experts):
    route = jnp.sum((chosen == 0).astype(jnp.float32), axis=1)
    partner = jnp.minimum(jnp.sum(chosen, axis=1), experts - 1)
    labels = jnp.arange(experts, dtype=jnp.int32)
    onehot = (partner[:, None] == labels[None, :]).astype(jnp.float32)
    wide_logits = logits.astype(jnp.float32)
    sigma = jax.nn.sigmoid(wide_logits[:, 0] - jnp.sum(wide_logits * onehot, axis=1))
    return (route, onehot, sigma, route * sigma)


def shards(x_fwd, act_fwd, ids_fwd, x_bwd, act_bwd, ids_bwd, grad_out, gain, w_router, w_down):
    x_fwd, act_fwd, ids_fwd, x_bwd, act_bwd = (x_fwd[0], act_fwd[0], ids_fwd[0], x_bwd[0], act_bwd[0])
    ids_bwd, grad_out, gain, w_router, w_down = (ids_bwd[0], grad_out[0], gain[0], w_router[0], w_down[0])
    experts = w_router.shape[1]
    width = x_fwd.shape[1]
    own_rows = x_fwd.shape[0]
    groups = lax.axis_size("ety") * lax.axis_size("etc")
    first_row = (lax.axis_index("ety") * lax.axis_size("etc") + lax.axis_index("etc")) * own_rows
    pad = 128

    wide_f, inverse_f, logit_f = norm_logits(x_fwd, gain, w_router)
    backward_wide_rows, backward_inverse_norm, logit_b = norm_logits(x_bwd, gain, w_router)

    packed = jnp.concatenate(
        [grad_out, jnp.pad(logit_b, ((0, 0), (0, pad - experts)))], axis=1
    )
    chips = lax.axis_size("ety")
    core = lax.axis_index("etc")
    tiled = jnp.broadcast_to(packed[None], (chips,) + packed.shape).reshape(chips * own_rows, -1)
    same_core = lax.all_to_all(tiled, "ety", 0, 0, tiled=True).reshape(chips, 1, own_rows, -1)
    other_core = lax.ppermute(same_core, "etc", [(0, 1), (1, 0)])
    full = jnp.where(
        core == 0,
        jnp.concatenate([same_core, other_core], axis=1),
        jnp.concatenate([other_core, same_core], axis=1),
    ).reshape(groups * own_rows, -1)
    full_g = full[:, :width]
    full_b = full[:, width : width + experts]

    route_b, onehot_b, sigma_b, coef_b = routing(full_b, ids_bwd, experts)
    back_up = lax.dot_general(
        full_g, w_down, (((1,), (1,)), ((), ())), preferred_element_type=jnp.float32
    )
    dact = (coef_b[:, None] * back_up).astype(jnp.bfloat16)
    dprob_part = jnp.sum(act_bwd.astype(jnp.float32) * back_up, axis=1)
    dprob_hi = dprob_part.astype(jnp.bfloat16)
    dprob_lo = (dprob_part - dprob_hi.astype(jnp.float32)).astype(jnp.bfloat16)

    z_fwd = jnp.dot(act_fwd, w_down, preferred_element_type=jnp.float32).astype(jnp.bfloat16)
    z_fwd = z_fwd.reshape(chips, 2, own_rows, width)
    d_split = jnp.stack([dprob_hi, dprob_lo], axis=-1).reshape(chips, 2, own_rows, 2)
    mine_z = jnp.where(core == 0, z_fwd[:, 0], z_fwd[:, 1])
    give_z = jnp.where(core == 0, z_fwd[:, 1], z_fwd[:, 0])
    mine_d = jnp.where(core == 0, d_split[:, 0], d_split[:, 1])
    give_d = jnp.where(core == 0, d_split[:, 1], d_split[:, 0])
    given = lax.ppermute(
        jnp.concatenate([give_z, jnp.pad(give_d, ((0, 0), (0, 0), (0, pad - 2)))], axis=-1),
        "etc",
        [(0, 1), (1, 0)],
    )
    pair_z = (mine_z.astype(jnp.float32) + given[..., :width].astype(jnp.float32)).astype(jnp.bfloat16)
    pair_d = jnp.sum(mine_d.astype(jnp.float32), axis=-1) + jnp.sum(
        given[..., width : width + 2].astype(jnp.float32), axis=-1
    )
    pair_hi = pair_d.astype(jnp.bfloat16)
    pair_lo = (pair_d - pair_hi.astype(jnp.float32)).astype(jnp.bfloat16)
    extra = jnp.concatenate(
        [pair_hi[..., None], pair_lo[..., None], jnp.zeros((chips, own_rows, pad - 2), jnp.bfloat16)],
        axis=-1,
    )
    sent = jnp.concatenate([pair_z, extra], axis=-1).reshape(chips * own_rows, -1)
    got = lax.all_to_all(sent, "ety", 0, 0, tiled=True).reshape(chips, own_rows, -1)
    got = got.astype(jnp.float32)
    z_sum = jnp.sum(got[:, :, :width], axis=0)
    dprob_mine = jnp.sum(got[:, :, width] + got[:, :, width + 1], axis=0)

    ids_f_own = lax.dynamic_slice_in_dim(ids_fwd, first_row, own_rows, 0)
    _, _, _, coef_f = routing(logit_f, ids_f_own, experts)
    layer_out = (wide_f + coef_f[:, None] * z_sum).astype(jnp.bfloat16)

    ids_b_own = lax.dynamic_slice_in_dim(ids_bwd, first_row, own_rows, 0)
    route_mine, onehot_mine, sigma_mine, _ = routing(logit_b, ids_b_own, experts)
    slope = route_mine * dprob_mine * sigma_mine * (1.0 - sigma_mine)
    router_wide = w_router.astype(jnp.float32)
    spread = router_wide[:, 0][None, :] - jnp.dot(
        onehot_mine, router_wide.T, precision=lax.Precision.HIGHEST
    )
    dnormed = slope[:, None] * spread
    scaled_rows = dnormed * gain.astype(jnp.float32)
    normalized_input = backward_wide_rows * backward_inverse_norm
    norm_input_gradient = backward_inverse_norm * (
        scaled_rows
        - normalized_input * jnp.mean(scaled_rows * normalized_input, axis=-1, keepdims=True)
    )
    input_grad = (grad_out.astype(jnp.float32) + norm_input_gradient).astype(jnp.bfloat16)
    fwd_in = from_behind(layer_out, "section", 1)
    incoming_gradient = from_behind(input_grad, "section", -1)
    return (fwd_in[None], incoming_gradient[None], dact[None])


def solution(mesh):
    sections, ets = mesh.devices.shape
    mesh = jax.sharding.Mesh(mesh.devices.reshape(sections, ets // 2, 2), ("section", "ety", "etc"))
    et = ("ety", "etc")
    placed = (
        P("section", et, None),
        P("section", None, et),
        P("section", None, None),
        P("section", et, None),
        P("section", None, et),
        P("section", None, None),
        P("section", et, None),
        P("section", None),
        P("section", None, None),
        P("section", et, None),
    )
    return jax.shard_map(
        shards,
        mesh=mesh,
        in_specs=placed,
        out_specs=(P("section", et, None), P("section", et, None), P("section", None, et)),
        check_vma=False,
    )
```

```python
import jax
import jax.numpy as jnp
from jax import lax
from jax.sharding import PartitionSpec as P


def from_behind(value, axis, steps):
    count = lax.axis_size(axis)
    first, last = (max(0, -steps), min(count, count - steps))
    return lax.ppermute(value, axis, [(source, source + steps) for source in range(first, last)])


def norm_logits(inputs, gain, w_router):
    wide = inputs.astype(jnp.float32)
    inverse = lax.rsqrt(jnp.mean(wide * wide, axis=-1, keepdims=True) + 1e-05)
    normed = (wide * inverse * gain.astype(jnp.float32)).astype(jnp.bfloat16)
    logits = jnp.dot(normed, w_router, preferred_element_type=jnp.float32).astype(jnp.bfloat16)
    return (wide, inverse, logits)


def routing(logits, chosen, experts):
    route = jnp.sum((chosen == 0).astype(jnp.float32), axis=1)
    partner = jnp.minimum(jnp.sum(chosen, axis=1), experts - 1)
    labels = jnp.arange(experts, dtype=jnp.int32)
    onehot = (partner[:, None] == labels[None, :]).astype(jnp.float32)
    wide_logits = logits.astype(jnp.float32)
    sigma = jax.nn.sigmoid(wide_logits[:, 0] - jnp.sum(wide_logits * onehot, axis=1))
    return (route, onehot, sigma, route * sigma)


def shards(x_fwd, act_fwd, ids_fwd, x_bwd, act_bwd, ids_bwd, grad_out, gain, w_router, w_down):
    x_fwd, act_fwd, ids_fwd, x_bwd, act_bwd = (x_fwd[0], act_fwd[0], ids_fwd[0], x_bwd[0], act_bwd[0])
    ids_bwd, grad_out, gain, w_router, w_down = (ids_bwd[0], grad_out[0], gain[0], w_router[0], w_down[0])
    experts = w_router.shape[1]
    width = x_fwd.shape[1]
    own_rows = x_fwd.shape[0]
    groups = lax.axis_size("ety") * lax.axis_size("etc")
    first_row = (lax.axis_index("ety") * lax.axis_size("etc") + lax.axis_index("etc")) * own_rows
    pad = 128

    wide_f, inverse_f, logit_f = norm_logits(x_fwd, gain, w_router)
    backward_wide_rows, backward_inverse_norm, logit_b = norm_logits(x_bwd, gain, w_router)

    packed = jnp.concatenate(
        [grad_out, jnp.pad(logit_b, ((0, 0), (0, pad - experts)))], axis=1
    )
    chips = lax.axis_size("ety")
    core = lax.axis_index("etc")
    tiled = jnp.broadcast_to(packed[None], (chips,) + packed.shape).reshape(chips * own_rows, -1)
    same_core = lax.all_to_all(tiled, "ety", 0, 0, tiled=True).reshape(chips, 1, own_rows, -1)
    other_core = lax.ppermute(same_core, "etc", [(0, 1), (1, 0)])
    full = jnp.where(
        core == 0,
        jnp.concatenate([same_core, other_core], axis=1),
        jnp.concatenate([other_core, same_core], axis=1),
    ).reshape(groups * own_rows, -1)
    full_g = full[:, :width]
    full_b = full[:, width : width + experts]

    route_b, onehot_b, sigma_b, coef_b = routing(full_b, ids_bwd, experts)
    back_up = lax.dot_general(
        full_g, w_down, (((1,), (1,)), ((), ())), preferred_element_type=jnp.float32
    )
    dact = (coef_b[:, None] * back_up).astype(jnp.bfloat16)
    dprob_part = jnp.sum(act_bwd.astype(jnp.float32) * back_up, axis=1)
    dprob_got = lax.all_to_all(dprob_part.reshape(groups, own_rows), ("ety", "etc"), 0, 0, tiled=True)
    dprob_mine = jnp.sum(dprob_got, axis=0)

    z_fwd = jnp.dot(act_fwd, w_down, preferred_element_type=jnp.float32).astype(jnp.bfloat16)
    z_fwd = z_fwd.reshape(chips, 2, own_rows, width)
    mine_z = jnp.where(core == 0, z_fwd[:, 0], z_fwd[:, 1])
    give_z = jnp.where(core == 0, z_fwd[:, 1], z_fwd[:, 0])
    given = lax.ppermute(give_z, "etc", [(0, 1), (1, 0)])
    pair_z = (mine_z.astype(jnp.float32) + given.astype(jnp.float32)).astype(jnp.bfloat16)
    got = lax.all_to_all(pair_z.reshape(chips * own_rows, width), "ety", 0, 0, tiled=True)
    z_sum = jnp.sum(got.reshape(chips, own_rows, width).astype(jnp.float32), axis=0)

    ids_f_own = lax.dynamic_slice_in_dim(ids_fwd, first_row, own_rows, 0)
    _, _, _, coef_f = routing(logit_f, ids_f_own, experts)
    layer_out = (wide_f + coef_f[:, None] * z_sum).astype(jnp.bfloat16)

    ids_b_own = lax.dynamic_slice_in_dim(ids_bwd, first_row, own_rows, 0)
    route_mine, onehot_mine, sigma_mine, _ = routing(logit_b, ids_b_own, experts)
    slope = route_mine * dprob_mine * sigma_mine * (1.0 - sigma_mine)
    router_wide = w_router.astype(jnp.float32)
    spread = router_wide[:, 0][None, :] - jnp.dot(
        onehot_mine, router_wide.T, precision=lax.Precision.HIGHEST
    )
    dnormed = slope[:, None] * spread
    scaled_rows = dnormed * gain.astype(jnp.float32)
    normalized_input = backward_wide_rows * backward_inverse_norm
    norm_input_gradient = backward_inverse_norm * (
        scaled_rows
        - normalized_input * jnp.mean(scaled_rows * normalized_input, axis=-1, keepdims=True)
    )
    input_grad = (grad_out.astype(jnp.float32) + norm_input_gradient).astype(jnp.bfloat16)
    fwd_in = from_behind(layer_out, "section", 1)
    incoming_gradient = from_behind(input_grad, "section", -1)
    return (fwd_in[None], incoming_gradient[None], dact[None])


def solution(mesh):
    sections, ets = mesh.devices.shape
    mesh = jax.sharding.Mesh(mesh.devices.reshape(sections, ets // 2, 2), ("section", "ety", "etc"))
    et = ("ety", "etc")
    placed = (
        P("section", et, None),
        P("section", None, et),
        P("section", None, None),
        P("section", et, None),
        P("section", None, et),
        P("section", None, None),
        P("section", et, None),
        P("section", None),
        P("section", None, None),
        P("section", et, None),
    )
    return jax.shard_map(
        shards,
        mesh=mesh,
        in_specs=placed,
        out_specs=(P("section", et, None), P("section", et, None), P("section", None, et)),
        check_vma=False,
    )
```

```python
import jax
import jax.numpy as jnp
from jax import lax
from jax.sharding import PartitionSpec as P


def from_behind(value, axis, steps):
    count = lax.axis_size(axis)
    first, last = (max(0, -steps), min(count, count - steps))
    return lax.ppermute(value, axis, [(source, source + steps) for source in range(first, last)])


def norm_logits(inputs, gain, w_router):
    wide = inputs.astype(jnp.float32)
    inverse = lax.rsqrt(jnp.mean(wide * wide, axis=-1, keepdims=True) + 1e-05)
    normed = (wide * inverse * gain.astype(jnp.float32)).astype(jnp.bfloat16)
    logits = jnp.dot(normed, w_router, preferred_element_type=jnp.float32).astype(jnp.bfloat16)
    return (wide, inverse, logits)


def routing(logits, chosen, experts):
    route = jnp.sum((chosen == 0).astype(jnp.float32), axis=1)
    partner = jnp.minimum(jnp.sum(chosen, axis=1), experts - 1)
    labels = jnp.arange(experts, dtype=jnp.int32)
    onehot = (partner[:, None] == labels[None, :]).astype(jnp.float32)
    wide_logits = logits.astype(jnp.float32)
    sigma = jax.nn.sigmoid(wide_logits[:, 0] - jnp.sum(wide_logits * onehot, axis=1))
    return (route, onehot, sigma, route * sigma)


def shards(x_fwd, act_fwd, ids_fwd, x_bwd, act_bwd, ids_bwd, grad_out, gain, w_router, w_down):
    x_fwd, act_fwd, ids_fwd, x_bwd, act_bwd = (x_fwd[0], act_fwd[0], ids_fwd[0], x_bwd[0], act_bwd[0])
    ids_bwd, grad_out, gain, w_router, w_down = (ids_bwd[0], grad_out[0], gain[0], w_router[0], w_down[0])
    experts = w_router.shape[1]
    width = x_fwd.shape[1]
    own_rows = x_fwd.shape[0]
    groups = lax.axis_size("ety") * lax.axis_size("etc")
    first_row = (lax.axis_index("ety") * lax.axis_size("etc") + lax.axis_index("etc")) * own_rows
    pad = 128

    wide_f, inverse_f, logit_f = norm_logits(x_fwd, gain, w_router)
    backward_wide_rows, backward_inverse_norm, logit_b = norm_logits(x_bwd, gain, w_router)

    packed = jnp.concatenate(
        [grad_out, jnp.pad(logit_b, ((0, 0), (0, pad - experts)))], axis=1
    )
    chips = lax.axis_size("ety")
    core = lax.axis_index("etc")
    tiled = jnp.broadcast_to(packed[None], (chips,) + packed.shape).reshape(chips * own_rows, -1)
    same_core = lax.all_to_all(tiled, "ety", 0, 0, tiled=True).reshape(chips, 1, own_rows, -1)
    z_fwd = jnp.dot(act_fwd, w_down, preferred_element_type=jnp.float32).astype(jnp.bfloat16)
    z_fwd = z_fwd.reshape(chips, 2, own_rows, width)
    mine_z = jnp.where(core == 0, z_fwd[:, 0], z_fwd[:, 1])
    give_z = jnp.where(core == 0, z_fwd[:, 1], z_fwd[:, 0])
    given = lax.ppermute(give_z, "etc", [(0, 1), (1, 0)])
    pair_z = (mine_z.astype(jnp.float32) + given.astype(jnp.float32)).astype(jnp.bfloat16)
    pair_z, same_core = lax.optimization_barrier((pair_z, same_core))
    got = lax.all_to_all(pair_z.reshape(chips * own_rows, width), "ety", 0, 0, tiled=True)
    z_sum = jnp.sum(got.reshape(chips, own_rows, width).astype(jnp.float32), axis=0)

    other_core = lax.ppermute(same_core, "etc", [(0, 1), (1, 0)])
    full = jnp.where(
        core == 0,
        jnp.concatenate([same_core, other_core], axis=1),
        jnp.concatenate([other_core, same_core], axis=1),
    ).reshape(groups * own_rows, -1)
    full_g = full[:, :width]
    full_b = full[:, width : width + experts]

    route_b, onehot_b, sigma_b, coef_b = routing(full_b, ids_bwd, experts)
    back_up = lax.dot_general(
        full_g, w_down, (((1,), (1,)), ((), ())), preferred_element_type=jnp.float32
    )
    dact = (coef_b[:, None] * back_up).astype(jnp.bfloat16)
    dprob_part = jnp.sum(act_bwd.astype(jnp.float32) * back_up, axis=1)
    dprob_part, z_sum = lax.optimization_barrier((dprob_part, z_sum))
    dprob_got = lax.all_to_all(dprob_part.reshape(groups, own_rows), ("ety", "etc"), 0, 0, tiled=True)
    dprob_mine = jnp.sum(dprob_got, axis=0)

    ids_f_own = lax.dynamic_slice_in_dim(ids_fwd, first_row, own_rows, 0)
    _, _, _, coef_f = routing(logit_f, ids_f_own, experts)
    layer_out = (wide_f + coef_f[:, None] * z_sum).astype(jnp.bfloat16)

    ids_b_own = lax.dynamic_slice_in_dim(ids_bwd, first_row, own_rows, 0)
    route_mine, onehot_mine, sigma_mine, _ = routing(logit_b, ids_b_own, experts)
    slope = route_mine * dprob_mine * sigma_mine * (1.0 - sigma_mine)
    router_wide = w_router.astype(jnp.float32)
    spread = router_wide[:, 0][None, :] - jnp.dot(
        onehot_mine, router_wide.T, precision=lax.Precision.HIGHEST
    )
    dnormed = slope[:, None] * spread
    scaled_rows = dnormed * gain.astype(jnp.float32)
    normalized_input = backward_wide_rows * backward_inverse_norm
    norm_input_gradient = backward_inverse_norm * (
        scaled_rows
        - normalized_input * jnp.mean(scaled_rows * normalized_input, axis=-1, keepdims=True)
    )
    input_grad = (grad_out.astype(jnp.float32) + norm_input_gradient).astype(jnp.bfloat16)
    fwd_in = from_behind(layer_out, "section", 1)
    incoming_gradient = from_behind(input_grad, "section", -1)
    return (fwd_in[None], incoming_gradient[None], dact[None])


def solution(mesh):
    sections, ets = mesh.devices.shape
    mesh = jax.sharding.Mesh(mesh.devices.reshape(sections, ets // 2, 2), ("section", "ety", "etc"))
    et = ("ety", "etc")
    placed = (
        P("section", et, None),
        P("section", None, et),
        P("section", None, None),
        P("section", et, None),
        P("section", None, et),
        P("section", None, None),
        P("section", et, None),
        P("section", None),
        P("section", None, None),
        P("section", et, None),
    )
    return jax.shard_map(
        shards,
        mesh=mesh,
        in_specs=placed,
        out_specs=(P("section", et, None), P("section", et, None), P("section", None, et)),
        check_vma=False,
    )
```

```python
import jax
import jax.numpy as jnp
from jax import lax
from jax.sharding import PartitionSpec as P


def from_behind(value, axis, steps):
    count = lax.axis_size(axis)
    first, last = (max(0, -steps), min(count, count - steps))
    return lax.ppermute(value, axis, [(source, source + steps) for source in range(first, last)])


def norm_logits(inputs, gain, w_router):
    wide = inputs.astype(jnp.float32)
    inverse = lax.rsqrt(jnp.mean(wide * wide, axis=-1, keepdims=True) + 1e-05)
    normed = (wide * inverse * gain.astype(jnp.float32)).astype(jnp.bfloat16)
    logits = jnp.dot(normed, w_router, preferred_element_type=jnp.float32).astype(jnp.bfloat16)
    return (wide, inverse, logits)


def routing(logits, chosen, experts):
    route = jnp.sum((chosen == 0).astype(jnp.float32), axis=1)
    partner = jnp.minimum(jnp.sum(chosen, axis=1), experts - 1)
    labels = jnp.arange(experts, dtype=jnp.int32)
    onehot = (partner[:, None] == labels[None, :]).astype(jnp.float32)
    wide_logits = logits.astype(jnp.float32)
    sigma = jax.nn.sigmoid(wide_logits[:, 0] - jnp.sum(wide_logits * onehot, axis=1))
    return (route, onehot, sigma, route * sigma)


def layer(x_fwd, act_fwd, ids_fwd, x_bwd, act_bwd, ids_bwd, grad_out, gain, w_router, w_down):
    x_fwd, act_fwd, ids_fwd, x_bwd, act_bwd = (x_fwd[0], act_fwd[0], ids_fwd[0], x_bwd[0], act_bwd[0])
    ids_bwd, grad_out, gain, w_router, w_down = (ids_bwd[0], grad_out[0], gain[0], w_router[0], w_down[0])
    experts = w_router.shape[1]
    width = x_fwd.shape[1]
    own_rows = x_fwd.shape[0]
    groups = lax.axis_size("ety") * lax.axis_size("etc")
    first_row = (lax.axis_index("ety") * lax.axis_size("etc") + lax.axis_index("etc")) * own_rows
    pad = 128

    wide_f, _, logit_f = norm_logits(x_fwd, gain, w_router)
    backward_wide_rows, backward_inverse_norm, logit_b = norm_logits(x_bwd, gain, w_router)

    packed = jnp.concatenate(
        [grad_out, jnp.pad(logit_b, ((0, 0), (0, pad - experts)))], axis=1
    )
    chips = lax.axis_size("ety")
    core = lax.axis_index("etc")
    tiled = jnp.broadcast_to(packed[None], (chips,) + packed.shape).reshape(chips * own_rows, -1)
    same_core = lax.all_to_all(tiled, "ety", 0, 0, tiled=True).reshape(chips, 1, own_rows, -1)
    z_fwd = jnp.dot(act_fwd, w_down, preferred_element_type=jnp.float32).astype(jnp.bfloat16)
    z_fwd = z_fwd.reshape(chips, 2, own_rows, width)
    mine_z = jnp.where(core == 0, z_fwd[:, 0], z_fwd[:, 1])
    give_z = jnp.where(core == 0, z_fwd[:, 1], z_fwd[:, 0])
    given = lax.ppermute(give_z, "etc", [(0, 1), (1, 0)])
    pair_z = (mine_z.astype(jnp.float32) + given.astype(jnp.float32)).astype(jnp.bfloat16)
    pair_z, same_core = lax.optimization_barrier((pair_z, same_core))
    got = lax.all_to_all(pair_z.reshape(chips * own_rows, width), "ety", 0, 0, tiled=True)
    z_sum = jnp.sum(got.reshape(chips, own_rows, width).astype(jnp.float32), axis=0)

    other_core = lax.ppermute(same_core, "etc", [(0, 1), (1, 0)])
    full = jnp.where(
        core == 0,
        jnp.concatenate([same_core, other_core], axis=1),
        jnp.concatenate([other_core, same_core], axis=1),
    ).reshape(groups * own_rows, -1)
    full_g = full[:, :width]
    full_b = full[:, width : width + experts]

    _, _, _, coef_b = routing(full_b, ids_bwd, experts)
    back_up = lax.dot_general(
        full_g, w_down, (((1,), (1,)), ((), ())), preferred_element_type=jnp.float32
    )
    dact = (coef_b[:, None] * back_up).astype(jnp.bfloat16)
    dprob_part = jnp.sum(act_bwd.astype(jnp.float32) * back_up, axis=1)
    halves = dprob_part.reshape(chips, 2, own_rows)
    keep = jnp.where(core == 0, halves[:, 0], halves[:, 1])
    give = jnp.where(core == 0, halves[:, 1], halves[:, 0])
    dprob_left = keep + lax.ppermute(give, "etc", [(0, 1), (1, 0)])
    chip = lax.axis_index("ety")
    span = chips // 2
    while span >= 1:
        bit = (chip // span) % 2
        split = dprob_left.reshape(2, -1, own_rows)
        keep = jnp.where(bit == 0, split[0], split[1])
        give = jnp.where(bit == 0, split[1], split[0])
        dprob_left = keep + lax.ppermute(give, "ety", [(i, i ^ span) for i in range(chips)])
        span //= 2
    dprob_mine = dprob_left.reshape(own_rows) + 0.0

    ids_f_own = lax.dynamic_slice_in_dim(ids_fwd, first_row, own_rows, 0)
    _, _, _, coef_f = routing(logit_f, ids_f_own, experts)
    layer_out = (wide_f + coef_f[:, None] * z_sum).astype(jnp.bfloat16)

    ids_b_own = lax.dynamic_slice_in_dim(ids_bwd, first_row, own_rows, 0)
    route_mine, onehot_mine, sigma_mine, _ = routing(logit_b, ids_b_own, experts)
    router_wide = w_router.astype(jnp.float32)
    spread = router_wide[:, 0][None, :] - jnp.dot(
        onehot_mine, router_wide.T, precision=lax.Precision.HIGHEST
    )
    scaled_rows = spread * gain.astype(jnp.float32)
    normalized_input = backward_wide_rows * backward_inverse_norm
    along = (route_mine * sigma_mine * (1.0 - sigma_mine))[:, None] * backward_inverse_norm * (
        scaled_rows
        - normalized_input * jnp.mean(scaled_rows * normalized_input, axis=-1, keepdims=True)
    )
    norm_input_gradient = dprob_mine[:, None] * along
    input_grad = (grad_out.astype(jnp.float32) + norm_input_gradient).astype(jnp.bfloat16)
    fwd_in = from_behind(layer_out, "section", 1)
    incoming_gradient = from_behind(input_grad, "section", -1)
    return (fwd_in[None], incoming_gradient[None], dact[None])


def solution(mesh):
    sections, ets = mesh.devices.shape
    mesh = jax.sharding.Mesh(mesh.devices.reshape(sections, ets // 2, 2), ("section", "ety", "etc"))
    et = ("ety", "etc")
    placed = (
        P("section", et, None),
        P("section", None, et),
        P("section", None, None),
        P("section", et, None),
        P("section", None, et),
        P("section", None, None),
        P("section", et, None),
        P("section", None),
        P("section", None, None),
        P("section", et, None),
    )
    return jax.shard_map(
        layer,
        mesh=mesh,
        in_specs=placed,
        out_specs=(P("section", et, None), P("section", et, None), P("section", None, et)),
        check_vma=False,
    )
```

```python
import jax
import jax.numpy as jnp
from jax import lax
from jax.sharding import PartitionSpec as P


def from_behind(value, axis, steps):
    count = lax.axis_size(axis)
    first, last = (max(0, -steps), min(count, count - steps))
    return lax.ppermute(value, axis, [(source, source + steps) for source in range(first, last)])


def norm_logits(inputs, gain, w_router):
    wide = inputs.astype(jnp.float32)
    inverse = lax.rsqrt(jnp.mean(wide * wide, axis=-1, keepdims=True) + 1e-05)
    normed = (wide * inverse * gain.astype(jnp.float32)).astype(jnp.bfloat16)
    logits = jnp.dot(normed, w_router, preferred_element_type=jnp.float32).astype(jnp.bfloat16)
    return (wide, inverse, logits)


def routing(logits, chosen, experts):
    route = jnp.sum((chosen == 0).astype(jnp.float32), axis=1)
    partner = jnp.minimum(jnp.sum(chosen, axis=1), experts - 1)
    labels = jnp.arange(experts, dtype=jnp.int32)
    onehot = (partner[:, None] == labels[None, :]).astype(jnp.float32)
    wide_logits = logits.astype(jnp.float32)
    sigma = jax.nn.sigmoid(wide_logits[:, 0] - jnp.sum(wide_logits * onehot, axis=1))
    return (route, onehot, sigma, route * sigma)


def layer(x_fwd, act_fwd, ids_fwd, x_bwd, act_bwd, ids_bwd, grad_out, gain, w_router, w_down):
    x_fwd, act_fwd, ids_fwd, x_bwd, act_bwd = (x_fwd[0], act_fwd[0], ids_fwd[0], x_bwd[0], act_bwd[0])
    ids_bwd, grad_out, gain, w_router, w_down = (ids_bwd[0], grad_out[0], gain[0], w_router[0], w_down[0])
    experts = w_router.shape[1]
    width = x_fwd.shape[1]
    own_rows = x_fwd.shape[0]
    hidden = w_down.shape[0]
    chips = lax.axis_size("ety")
    core = lax.axis_index("etc")
    swap = [(0, 1), (1, 0)]
    first_row = (lax.axis_index("ety") * 2 + core) * own_rows
    pad = 128

    def by_core(mine, other):
        return jnp.where(
            core == 0, jnp.stack([mine, other], axis=1), jnp.stack([other, mine], axis=1)
        )

    tiled = jnp.broadcast_to(grad_out[None], (chips,) + grad_out.shape)
    same_g = lax.all_to_all(tiled.reshape(chips * own_rows, width), "ety", 0, 0, tiled=True)
    other_g = lax.ppermute(same_g, "etc", swap)

    wide_f, _, logit_f = norm_logits(x_fwd, gain, w_router)
    backward_wide_rows, backward_inverse_norm, logit_b = norm_logits(x_bwd, gain, w_router)
    logit_pad = jnp.pad(logit_b, ((0, 0), (0, pad - experts)))

    z_fwd = jnp.dot(act_fwd, w_down, preferred_element_type=jnp.float32).astype(jnp.bfloat16)
    z_fwd = z_fwd.reshape(chips, 2, own_rows, width)
    mine_z = jnp.where(core == 0, z_fwd[:, 0], z_fwd[:, 1])
    give_z = jnp.where(core == 0, z_fwd[:, 1], z_fwd[:, 0])
    given = lax.ppermute(
        jnp.concatenate([give_z, jnp.broadcast_to(logit_pad[None], (chips, own_rows, pad))], axis=-1),
        "etc",
        swap,
    )
    pair_z = (mine_z.astype(jnp.float32) + given[..., :width].astype(jnp.float32)).astype(jnp.bfloat16)
    partner_logits = given[0, :, width : width + experts]

    act_halves = act_bwd.reshape(chips, 2, own_rows, hidden)
    act_same = jnp.where(core == 0, act_halves[:, 0], act_halves[:, 1])
    act_other = jnp.where(core == 0, act_halves[:, 1], act_halves[:, 0])

    def up_of(rows):
        return lax.dot_general(
            rows, w_down, (((1,), (1,)), ((), ())), preferred_element_type=jnp.float32
        ).reshape(chips, own_rows, hidden)

    up_same = up_of(same_g)
    up_other = up_of(other_g)
    dp_same = jnp.sum(act_same.astype(jnp.float32) * up_same, axis=-1)
    dp_other = jnp.sum(act_other.astype(jnp.float32) * up_other, axis=-1)
    dprob_part = by_core(dp_same, dp_other)
    dprob_hi = dprob_part.astype(jnp.bfloat16)
    dprob_lo = (dprob_part - dprob_hi.astype(jnp.float32)).astype(jnp.bfloat16)
    extra = jnp.concatenate(
        [
            dprob_hi[:, 0, :, None],
            dprob_lo[:, 0, :, None],
            dprob_hi[:, 1, :, None],
            dprob_lo[:, 1, :, None],
            jnp.broadcast_to(logit_b[None], (chips, own_rows, experts)),
            jnp.broadcast_to(partner_logits[None], (chips, own_rows, experts)),
            jnp.zeros((chips, own_rows, pad - 4 - 2 * experts), jnp.bfloat16),
        ],
        axis=-1,
    )

    sent = jnp.concatenate([pair_z, extra], axis=-1).reshape(chips * own_rows, width + pad)
    got = lax.all_to_all(sent, "ety", 0, 0, tiled=True).reshape(chips, own_rows, width + pad)
    z_sum = jnp.sum(got[..., :width].astype(jnp.float32), axis=0)
    tail = got[..., width:].astype(jnp.float32)
    d_core0 = jnp.sum(tail[..., 0] + tail[..., 1], axis=0)
    d_core1 = jnp.sum(tail[..., 2] + tail[..., 3], axis=0)
    d_mine = jnp.where(core == 0, d_core0, d_core1)
    d_partner = jnp.where(core == 0, d_core1, d_core0)
    dprob_mine = d_mine + lax.ppermute(d_partner, "etc", swap)

    ids_f_own = lax.dynamic_slice_in_dim(ids_fwd, first_row, own_rows, 0)
    _, _, _, coef_f = routing(logit_f, ids_f_own, experts)
    layer_out = (wide_f + coef_f[:, None] * z_sum).astype(jnp.bfloat16)

    full_b = by_core(
        got[..., width + 4 : width + 4 + experts], got[..., width + 4 + experts : width + 4 + 2 * experts]
    ).reshape(chips * 2 * own_rows, experts)
    _, _, _, coef_b = routing(full_b, ids_bwd, experts)
    back_up = by_core(up_same, up_other).reshape(chips * 2 * own_rows, hidden)
    dact = (coef_b[:, None] * back_up).astype(jnp.bfloat16)

    ids_b_own = lax.dynamic_slice_in_dim(ids_bwd, first_row, own_rows, 0)
    route_mine, onehot_mine, sigma_mine, _ = routing(logit_b, ids_b_own, experts)
    router_wide = w_router.astype(jnp.float32)
    spread = router_wide[:, 0][None, :] - jnp.dot(
        onehot_mine, router_wide.T, precision=lax.Precision.HIGHEST
    )
    scaled_rows = spread * gain.astype(jnp.float32)
    normalized_input = backward_wide_rows * backward_inverse_norm
    along = (route_mine * sigma_mine * (1.0 - sigma_mine))[:, None] * backward_inverse_norm * (
        scaled_rows
        - normalized_input * jnp.mean(scaled_rows * normalized_input, axis=-1, keepdims=True)
    )
    norm_input_gradient = dprob_mine[:, None] * along
    input_grad = (grad_out.astype(jnp.float32) + norm_input_gradient).astype(jnp.bfloat16)
    fwd_in = from_behind(layer_out, "section", 1)
    incoming_gradient = from_behind(input_grad, "section", -1)
    return (fwd_in[None], incoming_gradient[None], dact[None])


def solution(mesh):
    sections, ets = mesh.devices.shape
    mesh = jax.sharding.Mesh(mesh.devices.reshape(sections, ets // 2, 2), ("section", "ety", "etc"))
    et = ("ety", "etc")
    placed = (
        P("section", et, None),
        P("section", None, et),
        P("section", None, None),
        P("section", et, None),
        P("section", None, et),
        P("section", None, None),
        P("section", et, None),
        P("section", None),
        P("section", None, None),
        P("section", et, None),
    )
    return jax.shard_map(
        layer,
        mesh=mesh,
        in_specs=placed,
        out_specs=(P("section", et, None), P("section", et, None), P("section", None, et)),
        check_vma=False,
    )
```

```python
import jax
import jax.numpy as jnp
from jax import lax
from jax.sharding import PartitionSpec as P


def from_behind(value, axis, steps):
    count = lax.axis_size(axis)
    first, last = (max(0, -steps), min(count, count - steps))
    return lax.ppermute(value, axis, [(source, source + steps) for source in range(first, last)])


def norm_logits(inputs, gain, w_router):
    wide = inputs.astype(jnp.float32)
    inverse = lax.rsqrt(jnp.mean(wide * wide, axis=-1, keepdims=True) + 1e-05)
    normed = (wide * inverse * gain.astype(jnp.float32)).astype(jnp.bfloat16)
    logits = jnp.dot(normed, w_router, preferred_element_type=jnp.float32).astype(jnp.bfloat16)
    return (wide, inverse, logits)


def routing(logits, chosen, experts):
    route = jnp.sum((chosen == 0).astype(jnp.float32), axis=1)
    partner = jnp.minimum(jnp.sum(chosen, axis=1), experts - 1)
    labels = jnp.arange(experts, dtype=jnp.int32)
    onehot = (partner[:, None] == labels[None, :]).astype(jnp.float32)
    wide_logits = logits.astype(jnp.float32)
    sigma = jax.nn.sigmoid(wide_logits[:, 0] - jnp.sum(wide_logits * onehot, axis=1))
    return (route, onehot, sigma, route * sigma)


def shards(x_fwd, act_fwd, ids_fwd, x_bwd, act_bwd, ids_bwd, grad_out, gain, w_router, w_down):
    x_fwd, act_fwd, ids_fwd, x_bwd, act_bwd = (x_fwd[0], act_fwd[0], ids_fwd[0], x_bwd[0], act_bwd[0])
    ids_bwd, grad_out, gain, w_router, w_down = (ids_bwd[0], grad_out[0], gain[0], w_router[0], w_down[0])
    experts = w_router.shape[1]
    width = x_fwd.shape[1]
    own_rows = x_fwd.shape[0]
    groups = lax.axis_size("ety") * lax.axis_size("etc")
    first_row = (lax.axis_index("ety") * lax.axis_size("etc") + lax.axis_index("etc")) * own_rows
    pad = 128

    wide_f, inverse_f, logit_f = norm_logits(x_fwd, gain, w_router)
    backward_wide_rows, backward_inverse_norm, logit_b = norm_logits(x_bwd, gain, w_router)

    packed = jnp.concatenate(
        [grad_out, jnp.pad(logit_b, ((0, 0), (0, pad - experts)))], axis=1
    )
    chips = lax.axis_size("ety")
    core = lax.axis_index("etc")
    tiled = jnp.broadcast_to(packed[None], (chips,) + packed.shape).reshape(chips * own_rows, -1)
    same_core = lax.all_to_all(tiled, "ety", 0, 0, tiled=True).reshape(chips, 1, own_rows, -1)
    z_fwd = jnp.dot(act_fwd, w_down, preferred_element_type=jnp.float32).astype(jnp.bfloat16)
    z_fwd = z_fwd.reshape(chips, 2, own_rows, width)
    mine_z = jnp.where(core == 0, z_fwd[:, 0], z_fwd[:, 1])
    give_z = jnp.where(core == 0, z_fwd[:, 1], z_fwd[:, 0])
    given = lax.ppermute(give_z, "etc", [(0, 1), (1, 0)])
    pair_z = (mine_z.astype(jnp.float32) + given.astype(jnp.float32)).astype(jnp.bfloat16)
    pair_z, same_core = lax.optimization_barrier((pair_z, same_core))
    cut = width // 2
    got_a = lax.all_to_all(pair_z[..., :cut].reshape(chips * own_rows, cut), "ety", 0, 0, tiled=True)

    other_core = lax.ppermute(same_core, "etc", [(0, 1), (1, 0)])
    full = jnp.where(
        core == 0,
        jnp.concatenate([same_core, other_core], axis=1),
        jnp.concatenate([other_core, same_core], axis=1),
    ).reshape(groups * own_rows, -1)
    full_g = full[:, :width]
    full_b = full[:, width : width + experts]

    route_b, onehot_b, sigma_b, coef_b = routing(full_b, ids_bwd, experts)
    back_up = lax.dot_general(
        full_g, w_down, (((1,), (1,)), ((), ())), preferred_element_type=jnp.float32
    )
    dact = (coef_b[:, None] * back_up).astype(jnp.bfloat16)
    dprob_part = jnp.sum(act_bwd.astype(jnp.float32) * back_up, axis=1)
    halves = dprob_part.reshape(chips, 2, own_rows)
    keep = jnp.where(core == 0, halves[:, 0], halves[:, 1])
    give = jnp.where(core == 0, halves[:, 1], halves[:, 0])
    pair_d = keep + lax.ppermute(give, "etc", [(0, 1), (1, 0)])
    pair_hi = pair_d.astype(jnp.bfloat16)
    pair_lo = (pair_d - pair_hi.astype(jnp.float32)).astype(jnp.bfloat16)
    extra = jnp.concatenate(
        [pair_hi[..., None], pair_lo[..., None], jnp.zeros((chips, own_rows, pad - 2), jnp.bfloat16)],
        axis=-1,
    )
    sent_b = jnp.concatenate([pair_z[..., cut:], extra], axis=-1)
    got_b = lax.all_to_all(
        sent_b.reshape(chips * own_rows, width - cut + pad), "ety", 0, 0, tiled=True
    ).reshape(chips, own_rows, -1)
    got_a = got_a.reshape(chips, own_rows, cut)
    z_sum = jnp.concatenate(
        [
            jnp.sum(got_a.astype(jnp.float32), axis=0),
            jnp.sum(got_b[..., : width - cut].astype(jnp.float32), axis=0),
        ],
        axis=-1,
    )
    tail = got_b[..., width - cut :].astype(jnp.float32)
    dprob_mine = jnp.sum(tail[..., 0] + tail[..., 1], axis=0)

    ids_f_own = lax.dynamic_slice_in_dim(ids_fwd, first_row, own_rows, 0)
    _, _, _, coef_f = routing(logit_f, ids_f_own, experts)
    layer_out = (wide_f + coef_f[:, None] * z_sum).astype(jnp.bfloat16)

    ids_b_own = lax.dynamic_slice_in_dim(ids_bwd, first_row, own_rows, 0)
    route_mine, onehot_mine, sigma_mine, _ = routing(logit_b, ids_b_own, experts)
    slope = route_mine * dprob_mine * sigma_mine * (1.0 - sigma_mine)
    router_wide = w_router.astype(jnp.float32)
    spread = router_wide[:, 0][None, :] - jnp.dot(
        onehot_mine, router_wide.T, precision=lax.Precision.HIGHEST
    )
    dnormed = slope[:, None] * spread
    scaled_rows = dnormed * gain.astype(jnp.float32)
    normalized_input = backward_wide_rows * backward_inverse_norm
    norm_input_gradient = backward_inverse_norm * (
        scaled_rows
        - normalized_input * jnp.mean(scaled_rows * normalized_input, axis=-1, keepdims=True)
    )
    input_grad = (grad_out.astype(jnp.float32) + norm_input_gradient).astype(jnp.bfloat16)
    fwd_in = from_behind(layer_out, "section", 1)
    incoming_gradient = from_behind(input_grad, "section", -1)
    return (fwd_in[None], incoming_gradient[None], dact[None])


def solution(mesh):
    sections, ets = mesh.devices.shape
    mesh = jax.sharding.Mesh(mesh.devices.reshape(sections, ets // 2, 2), ("section", "ety", "etc"))
    et = ("ety", "etc")
    placed = (
        P("section", et, None),
        P("section", None, et),
        P("section", None, None),
        P("section", et, None),
        P("section", None, et),
        P("section", None, None),
        P("section", et, None),
        P("section", None),
        P("section", None, None),
        P("section", et, None),
    )
    return jax.shard_map(
        shards,
        mesh=mesh,
        in_specs=placed,
        out_specs=(P("section", et, None), P("section", et, None), P("section", None, et)),
        check_vma=False,
    )
```

```python
import jax
import jax.numpy as jnp
from jax import lax
from jax.sharding import PartitionSpec as P


def from_behind(value, axis, steps):
    count = lax.axis_size(axis)
    first, last = (max(0, -steps), min(count, count - steps))
    return lax.ppermute(value, axis, [(source, source + steps) for source in range(first, last)])


def norm_logits(inputs, gain, w_router):
    wide = inputs.astype(jnp.float32)
    inverse = lax.rsqrt(jnp.mean(wide * wide, axis=-1, keepdims=True) + 1e-05)
    normed = (wide * inverse * gain.astype(jnp.float32)).astype(jnp.bfloat16)
    logits = jnp.dot(normed, w_router, preferred_element_type=jnp.float32).astype(jnp.bfloat16)
    return (wide, inverse, logits)


def routing(logits, chosen, experts):
    route = jnp.sum((chosen == 0).astype(jnp.float32), axis=1)
    partner = jnp.minimum(jnp.sum(chosen, axis=1), experts - 1)
    labels = jnp.arange(experts, dtype=jnp.int32)
    onehot = (partner[:, None] == labels[None, :]).astype(jnp.float32)
    wide_logits = logits.astype(jnp.float32)
    sigma = jax.nn.sigmoid(wide_logits[:, 0] - jnp.sum(wide_logits * onehot, axis=1))
    return (route, onehot, sigma, route * sigma)


def layer(x_fwd, act_fwd, ids_fwd, x_bwd, act_bwd, ids_bwd, grad_out, gain, w_router, w_down):
    x_fwd, act_fwd, ids_fwd, x_bwd, act_bwd = (x_fwd[0], act_fwd[0], ids_fwd[0], x_bwd[0], act_bwd[0])
    ids_bwd, grad_out, gain, w_router, w_down = (ids_bwd[0], grad_out[0], gain[0], w_router[0], w_down[0])
    experts = w_router.shape[1]
    width = x_fwd.shape[1]
    own_rows = x_fwd.shape[0]
    groups = lax.axis_size("ety") * lax.axis_size("etc")
    first_row = (lax.axis_index("ety") * lax.axis_size("etc") + lax.axis_index("etc")) * own_rows
    pad = 128

    chips = lax.axis_size("ety")
    core = lax.axis_index("etc")
    swap = [(0, 1), (1, 0)]

    def by_core(mine, other):
        return jnp.where(
            core == 0, jnp.stack([mine, other], axis=1), jnp.stack([other, mine], axis=1)
        )

    tiled = jnp.broadcast_to(grad_out[None], (chips,) + grad_out.shape)
    same_g = lax.all_to_all(tiled.reshape(chips * own_rows, width), "ety", 0, 0, tiled=True)

    wide_f, _, logit_f = norm_logits(x_fwd, gain, w_router)
    backward_wide_rows, backward_inverse_norm, logit_b = norm_logits(x_bwd, gain, w_router)
    logit_pad = jnp.pad(logit_b, ((0, 0), (0, pad - experts)))

    z_fwd = jnp.dot(act_fwd, w_down, preferred_element_type=jnp.float32).astype(jnp.bfloat16)
    z_fwd = z_fwd.reshape(chips, 2, own_rows, width)
    mine_z = jnp.where(core == 0, z_fwd[:, 0], z_fwd[:, 1])
    give_z = jnp.where(core == 0, z_fwd[:, 1], z_fwd[:, 0])
    given = lax.ppermute(
        jnp.concatenate([give_z, jnp.broadcast_to(logit_pad[None], (chips, own_rows, pad))], axis=-1),
        "etc",
        swap,
    )
    pair_z = (mine_z.astype(jnp.float32) + given[..., :width].astype(jnp.float32)).astype(jnp.bfloat16)
    partner_logits = given[0, :, width : width + experts]
    extra = jnp.concatenate(
        [
            jnp.broadcast_to(logit_b[None], (chips, own_rows, experts)),
            jnp.broadcast_to(partner_logits[None], (chips, own_rows, experts)),
            jnp.zeros((chips, own_rows, pad - 2 * experts), jnp.bfloat16),
        ],
        axis=-1,
    )
    sent = jnp.concatenate([pair_z, extra], axis=-1)
    sent, same_g = lax.optimization_barrier((sent, same_g))
    got = lax.all_to_all(sent.reshape(chips * own_rows, width + pad), "ety", 0, 0, tiled=True)
    got = got.reshape(chips, own_rows, width + pad)
    z_sum = jnp.sum(got[..., :width].astype(jnp.float32), axis=0)

    other_g = lax.ppermute(same_g, "etc", swap)
    full_g = by_core(same_g.reshape(chips, own_rows, width), other_g.reshape(chips, own_rows, width))
    back_up = lax.dot_general(
        full_g.reshape(groups * own_rows, width), w_down, (((1,), (1,)), ((), ())),
        preferred_element_type=jnp.float32,
    )
    dprob_part = jnp.sum(act_bwd.astype(jnp.float32) * back_up, axis=1)
    back_up, dprob_part = lax.optimization_barrier((back_up, dprob_part))
    dprob_part, z_sum = lax.optimization_barrier((dprob_part, z_sum))
    dprob_got = lax.all_to_all(dprob_part.reshape(groups, own_rows), ("ety", "etc"), 0, 0, tiled=True)
    dprob_mine = jnp.sum(dprob_got, axis=0)

    full_b = by_core(got[..., width : width + experts], got[..., width + experts : width + 2 * experts])
    _, _, _, coef_b = routing(full_b.reshape(groups * own_rows, experts), ids_bwd, experts)
    dact = (coef_b[:, None] * back_up).astype(jnp.bfloat16)

    ids_f_own = lax.dynamic_slice_in_dim(ids_fwd, first_row, own_rows, 0)
    _, _, _, coef_f = routing(logit_f, ids_f_own, experts)
    layer_out = (wide_f + coef_f[:, None] * z_sum).astype(jnp.bfloat16)

    ids_b_own = lax.dynamic_slice_in_dim(ids_bwd, first_row, own_rows, 0)
    route_mine, onehot_mine, sigma_mine, _ = routing(logit_b, ids_b_own, experts)
    slope = route_mine * dprob_mine * sigma_mine * (1.0 - sigma_mine)
    router_wide = w_router.astype(jnp.float32)
    spread = router_wide[:, 0][None, :] - jnp.dot(
        onehot_mine, router_wide.T, precision=lax.Precision.HIGHEST
    )
    dnormed = slope[:, None] * spread
    scaled_rows = dnormed * gain.astype(jnp.float32)
    normalized_input = backward_wide_rows * backward_inverse_norm
    norm_input_gradient = backward_inverse_norm * (
        scaled_rows
        - normalized_input * jnp.mean(scaled_rows * normalized_input, axis=-1, keepdims=True)
    )
    input_grad = (grad_out.astype(jnp.float32) + norm_input_gradient).astype(jnp.bfloat16)
    fwd_in = from_behind(layer_out, "section", 1)
    incoming_gradient = from_behind(input_grad, "section", -1)
    return (fwd_in[None], incoming_gradient[None], dact[None])


def solution(mesh):
    sections, ets = mesh.devices.shape
    mesh = jax.sharding.Mesh(mesh.devices.reshape(sections, ets // 2, 2), ("section", "ety", "etc"))
    et = ("ety", "etc")
    placed = (
        P("section", et, None),
        P("section", None, et),
        P("section", None, None),
        P("section", et, None),
        P("section", None, et),
        P("section", None, None),
        P("section", et, None),
        P("section", None),
        P("section", None, None),
        P("section", et, None),
    )
    return jax.shard_map(
        layer,
        mesh=mesh,
        in_specs=placed,
        out_specs=(P("section", et, None), P("section", et, None), P("section", None, et)),
        check_vma=False,
    )
```

```python
import jax
import jax.numpy as jnp
from jax import lax
from jax.sharding import PartitionSpec as P


def from_behind(value, axis, steps):
    count = lax.axis_size(axis)
    first, last = (max(0, -steps), min(count, count - steps))
    return lax.ppermute(value, axis, [(source, source + steps) for source in range(first, last)])


def norm_logits(inputs, gain, w_router):
    wide = inputs.astype(jnp.float32)
    inverse = lax.rsqrt(jnp.mean(wide * wide, axis=-1, keepdims=True) + 1e-05)
    normed = (wide * inverse * gain.astype(jnp.float32)).astype(jnp.bfloat16)
    logits = jnp.dot(normed, w_router, preferred_element_type=jnp.float32).astype(jnp.bfloat16)
    return (wide, inverse, logits)


def routing(logits, chosen, experts):
    route = jnp.sum((chosen == 0).astype(jnp.float32), axis=1)
    partner = jnp.minimum(jnp.sum(chosen, axis=1), experts - 1)
    labels = jnp.arange(experts, dtype=jnp.int32)
    onehot = (partner[:, None] == labels[None, :]).astype(jnp.float32)
    wide_logits = logits.astype(jnp.float32)
    sigma = jax.nn.sigmoid(wide_logits[:, 0] - jnp.sum(wide_logits * onehot, axis=1))
    return (route, onehot, sigma, route * sigma)


def shards(x_fwd, act_fwd, ids_fwd, x_bwd, act_bwd, ids_bwd, grad_out, gain, w_router, w_down):
    x_fwd, act_fwd, ids_fwd, x_bwd, act_bwd = (x_fwd[0], act_fwd[0], ids_fwd[0], x_bwd[0], act_bwd[0])
    ids_bwd, grad_out, gain, w_router, w_down = (ids_bwd[0], grad_out[0], gain[0], w_router[0], w_down[0])
    experts = w_router.shape[1]
    width = x_fwd.shape[1]
    own_rows = x_fwd.shape[0]
    groups = lax.axis_size("ety") * lax.axis_size("etc")
    first_row = (lax.axis_index("ety") * lax.axis_size("etc") + lax.axis_index("etc")) * own_rows
    pad = 128

    wide_f, inverse_f, logit_f = norm_logits(x_fwd, gain, w_router)
    backward_wide_rows, backward_inverse_norm, logit_b = norm_logits(x_bwd, gain, w_router)

    packed = jnp.concatenate(
        [grad_out, jnp.pad(logit_b, ((0, 0), (0, pad - experts)))], axis=1
    )
    chips = lax.axis_size("ety")
    core = lax.axis_index("etc")
    tiled = jnp.broadcast_to(packed[None], (chips,) + packed.shape).reshape(chips * own_rows, -1)
    same_core = lax.all_to_all(tiled, "ety", 0, 0, tiled=True).reshape(chips, 1, own_rows, -1)
    z_fwd = jnp.dot(act_fwd, w_down, preferred_element_type=jnp.float32).astype(jnp.bfloat16)
    z_fwd = z_fwd.reshape(chips, 2, own_rows, width)
    mine_z = jnp.where(core == 0, z_fwd[:, 0], z_fwd[:, 1])
    give_z = jnp.where(core == 0, z_fwd[:, 1], z_fwd[:, 0])
    given = lax.ppermute(give_z, "etc", [(0, 1), (1, 0)])
    pair_z = (mine_z.astype(jnp.float32) + given.astype(jnp.float32)).astype(jnp.bfloat16)
    pair_z, same_core = lax.optimization_barrier((pair_z, same_core))
    got = lax.all_to_all(pair_z.reshape(chips * own_rows, width), "ety", 0, 0, tiled=True)

    other_core = lax.ppermute(same_core, "etc", [(0, 1), (1, 0)])
    full = jnp.where(
        core == 0,
        jnp.concatenate([same_core, other_core], axis=1),
        jnp.concatenate([other_core, same_core], axis=1),
    ).reshape(groups * own_rows, -1)
    full_g = full[:, :width]
    full_b = full[:, width : width + experts]

    route_b, onehot_b, sigma_b, coef_b = routing(full_b, ids_bwd, experts)
    back_up = lax.dot_general(
        full_g, w_down, (((1,), (1,)), ((), ())), preferred_element_type=jnp.float32
    )
    dact = (coef_b[:, None] * back_up).astype(jnp.bfloat16)
    dprob_part = jnp.sum(act_bwd.astype(jnp.float32) * back_up, axis=1)
    dprob_part, got = lax.optimization_barrier((dprob_part, got))
    dprob_got = lax.all_to_all(dprob_part.reshape(groups, own_rows), ("ety", "etc"), 0, 0, tiled=True)
    dprob_mine = jnp.sum(dprob_got, axis=0)
    z_sum = jnp.sum(got.reshape(chips, own_rows, width).astype(jnp.float32), axis=0)

    ids_f_own = lax.dynamic_slice_in_dim(ids_fwd, first_row, own_rows, 0)
    _, _, _, coef_f = routing(logit_f, ids_f_own, experts)
    layer_out = (wide_f + coef_f[:, None] * z_sum).astype(jnp.bfloat16)

    ids_b_own = lax.dynamic_slice_in_dim(ids_bwd, first_row, own_rows, 0)
    route_mine, onehot_mine, sigma_mine, _ = routing(logit_b, ids_b_own, experts)
    router_wide = w_router.astype(jnp.float32)
    spread = router_wide[:, 0][None, :] - jnp.dot(
        onehot_mine, router_wide.T, precision=lax.Precision.HIGHEST
    )
    scaled_rows = spread * gain.astype(jnp.float32)
    normalized_input = backward_wide_rows * backward_inverse_norm
    along = (route_mine * sigma_mine * (1.0 - sigma_mine))[:, None] * backward_inverse_norm * (
        scaled_rows
        - normalized_input * jnp.mean(scaled_rows * normalized_input, axis=-1, keepdims=True)
    )
    norm_input_gradient = dprob_mine[:, None] * along
    input_grad = (grad_out.astype(jnp.float32) + norm_input_gradient).astype(jnp.bfloat16)
    fwd_in = from_behind(layer_out, "section", 1)
    incoming_gradient = from_behind(input_grad, "section", -1)
    return (fwd_in[None], incoming_gradient[None], dact[None])


def solution(mesh):
    sections, ets = mesh.devices.shape
    mesh = jax.sharding.Mesh(mesh.devices.reshape(sections, ets // 2, 2), ("section", "ety", "etc"))
    et = ("ety", "etc")
    placed = (
        P("section", et, None),
        P("section", None, et),
        P("section", None, None),
        P("section", et, None),
        P("section", None, et),
        P("section", None, None),
        P("section", et, None),
        P("section", None),
        P("section", None, None),
        P("section", et, None),
    )
    return jax.shard_map(
        shards,
        mesh=mesh,
        in_specs=placed,
        out_specs=(P("section", et, None), P("section", et, None), P("section", None, et)),
        check_vma=False,
    )
```

```python
import jax
import jax.numpy as jnp
from jax import lax
from jax.sharding import PartitionSpec as P


def from_behind(value, axis, steps):
    count = lax.axis_size(axis)
    first, last = (max(0, -steps), min(count, count - steps))
    return lax.ppermute(value, axis, [(source, source + steps) for source in range(first, last)])


def norm_logits(inputs, gain, w_router):
    wide = inputs.astype(jnp.float32)
    inverse = lax.rsqrt(jnp.mean(wide * wide, axis=-1, keepdims=True) + 1e-05)
    normed = (wide * inverse * gain.astype(jnp.float32)).astype(jnp.bfloat16)
    logits = jnp.dot(normed, w_router, preferred_element_type=jnp.float32).astype(jnp.bfloat16)
    return (wide, inverse, logits)


def routing(logits, chosen, experts):
    route = jnp.sum((chosen == 0).astype(jnp.float32), axis=1)
    partner = jnp.minimum(jnp.sum(chosen, axis=1), experts - 1)
    labels = jnp.arange(experts, dtype=jnp.int32)
    onehot = (partner[:, None] == labels[None, :]).astype(jnp.float32)
    wide_logits = logits.astype(jnp.float32)
    sigma = jax.nn.sigmoid(wide_logits[:, 0] - jnp.sum(wide_logits * onehot, axis=1))
    return (route, onehot, sigma, route * sigma)


def layer(x_fwd, act_fwd, ids_fwd, x_bwd, act_bwd, ids_bwd, grad_out, gain, w_router, w_down):
    x_fwd, act_fwd, ids_fwd, x_bwd, act_bwd = (x_fwd[0], act_fwd[0], ids_fwd[0], x_bwd[0], act_bwd[0])
    ids_bwd, grad_out, gain, w_router, w_down = (ids_bwd[0], grad_out[0], gain[0], w_router[0], w_down[0])
    experts = w_router.shape[1]
    width = x_fwd.shape[1]
    own_rows = x_fwd.shape[0]
    groups = lax.axis_size("ety") * lax.axis_size("etc")
    first_row = (lax.axis_index("ety") * lax.axis_size("etc") + lax.axis_index("etc")) * own_rows
    pad = 128

    wide_f, _, logit_f = norm_logits(x_fwd, gain, w_router)
    backward_wide_rows, backward_inverse_norm, logit_b = norm_logits(x_bwd, gain, w_router)

    packed = jnp.concatenate(
        [grad_out, jnp.pad(logit_b, ((0, 0), (0, pad - experts)))], axis=1
    )
    chips = lax.axis_size("ety")
    core = lax.axis_index("etc")
    tiled = jnp.broadcast_to(packed[None], (chips,) + packed.shape).reshape(chips * own_rows, -1)
    same_core = lax.all_to_all(tiled, "ety", 0, 0, tiled=True).reshape(chips, 1, own_rows, -1)
    z_fwd = jnp.dot(act_fwd, w_down, preferred_element_type=jnp.float32).astype(jnp.bfloat16)
    z_fwd = z_fwd.reshape(chips, 2, own_rows, width)
    mine_z = jnp.where(core == 0, z_fwd[:, 0], z_fwd[:, 1])
    give_z = jnp.where(core == 0, z_fwd[:, 1], z_fwd[:, 0])
    given = lax.ppermute(give_z, "etc", [(0, 1), (1, 0)])
    pair_z = (mine_z.astype(jnp.float32) + given.astype(jnp.float32)).astype(jnp.bfloat16)
    pair_z, same_core = lax.optimization_barrier((pair_z, same_core))
    got = lax.all_to_all(pair_z.reshape(chips * own_rows, width), "ety", 0, 0, tiled=True)

    other_core = lax.ppermute(same_core, "etc", [(0, 1), (1, 0)])
    full = jnp.where(
        core == 0,
        jnp.concatenate([same_core, other_core], axis=1),
        jnp.concatenate([other_core, same_core], axis=1),
    ).reshape(groups * own_rows, -1)
    full_g = full[:, :width]
    full_b = full[:, width : width + experts]

    _, _, _, coef_b = routing(full_b, ids_bwd, experts)
    back_up = lax.dot_general(
        full_g, w_down, (((1,), (1,)), ((), ())), preferred_element_type=jnp.float32
    )
    dact = (coef_b[:, None] * back_up).astype(jnp.bfloat16)
    dprob_part = jnp.sum(act_bwd.astype(jnp.float32) * back_up, axis=1)
    dprob_part, got = lax.optimization_barrier((dprob_part, got))
    dprob_got = lax.all_to_all(dprob_part.reshape(groups, own_rows), ("ety", "etc"), 0, 0, tiled=True)
    dprob_mine = jnp.sum(dprob_got, axis=0)
    z_sum = jnp.sum(got.reshape(chips, own_rows, width).astype(jnp.float32), axis=0)

    ids_f_own = lax.dynamic_slice_in_dim(ids_fwd, first_row, own_rows, 0)
    _, _, _, coef_f = routing(logit_f, ids_f_own, experts)
    layer_out = (wide_f + coef_f[:, None] * z_sum).astype(jnp.bfloat16)

    ids_b_own = lax.dynamic_slice_in_dim(ids_bwd, first_row, own_rows, 0)
    route_mine, onehot_mine, sigma_mine, _ = routing(logit_b, ids_b_own, experts)
    router_wide = w_router.astype(jnp.float32)
    spread = router_wide[:, 0][None, :] - jnp.dot(
        onehot_mine, router_wide.T, precision=lax.Precision.HIGHEST
    )
    scaled_rows = spread * gain.astype(jnp.float32)
    normalized_input = backward_wide_rows * backward_inverse_norm
    along = (route_mine * sigma_mine * (1.0 - sigma_mine))[:, None] * backward_inverse_norm * (
        scaled_rows
        - normalized_input * jnp.mean(scaled_rows * normalized_input, axis=-1, keepdims=True)
    )
    norm_input_gradient = dprob_mine[:, None] * along
    input_grad = (grad_out.astype(jnp.float32) + norm_input_gradient).astype(jnp.bfloat16)
    fwd_in = from_behind(layer_out[None], "section", 1)
    incoming_gradient = from_behind(input_grad[None], "section", -1)
    return (fwd_in, incoming_gradient, dact[None])


def solution(mesh):
    sections, ets = mesh.devices.shape
    mesh = jax.sharding.Mesh(mesh.devices.reshape(sections, ets // 2, 2), ("section", "ety", "etc"))
    et = ("ety", "etc")
    placed = (
        P("section", et, None),
        P("section", None, et),
        P("section", None, None),
        P("section", et, None),
        P("section", None, et),
        P("section", None, None),
        P("section", et, None),
        P("section", None),
        P("section", None, None),
        P("section", et, None),
    )
    return jax.shard_map(
        layer,
        mesh=mesh,
        in_specs=placed,
        out_specs=(P("section", et, None), P("section", et, None), P("section", None, et)),
        check_vma=False,
    )
```

```python
import jax
import jax.numpy as jnp
from jax import lax
from jax.sharding import PartitionSpec as P


def from_behind(value, axis, steps):
    count = lax.axis_size(axis)
    first, last = (max(0, -steps), min(count, count - steps))
    return lax.ppermute(value, axis, [(source, source + steps) for source in range(first, last)])


def norm_logits(inputs, gain, w_router):
    wide = inputs.astype(jnp.float32)
    inverse = lax.rsqrt(jnp.mean(wide * wide, axis=-1, keepdims=True) + 1e-05)
    normed = (wide * inverse * gain.astype(jnp.float32)).astype(jnp.bfloat16)
    logits = jnp.dot(normed, w_router, preferred_element_type=jnp.float32).astype(jnp.bfloat16)
    return (wide, inverse, logits)


def routing(logits, chosen, experts):
    route = jnp.sum((chosen == 0).astype(jnp.float32), axis=1)
    partner = jnp.minimum(jnp.sum(chosen, axis=1), experts - 1)
    labels = jnp.arange(experts, dtype=jnp.int32)
    onehot = (partner[:, None] == labels[None, :]).astype(jnp.float32)
    wide_logits = logits.astype(jnp.float32)
    sigma = jax.nn.sigmoid(wide_logits[:, 0] - jnp.sum(wide_logits * onehot, axis=1))
    return (route, onehot, sigma, route * sigma)


def layer(x_fwd, act_fwd, ids_fwd, x_bwd, act_bwd, ids_bwd, grad_out, gain, w_router, w_down):
    x_fwd, act_fwd, ids_fwd, x_bwd, act_bwd = (x_fwd[0], act_fwd[0], ids_fwd[0], x_bwd[0], act_bwd[0])
    ids_bwd, grad_out, gain, w_router, w_down = (ids_bwd[0], grad_out[0], gain[0], w_router[0], w_down[0])
    experts = w_router.shape[1]
    width = x_fwd.shape[1]
    own_rows = x_fwd.shape[0]
    groups = lax.axis_size("ety") * lax.axis_size("etc")
    first_row = (lax.axis_index("ety") * lax.axis_size("etc") + lax.axis_index("etc")) * own_rows
    pad = 128

    wide_f, _, logit_f = norm_logits(x_fwd, gain, w_router)
    backward_wide_rows, backward_inverse_norm, logit_b = norm_logits(x_bwd, gain, w_router)

    packed = jnp.concatenate(
        [grad_out, jnp.pad(logit_b, ((0, 0), (0, pad - experts)))], axis=1
    )
    chips = lax.axis_size("ety")
    core = lax.axis_index("etc")
    tiled = jnp.broadcast_to(packed[None], (chips,) + packed.shape).reshape(chips * own_rows, -1)
    same_core = lax.all_to_all(tiled, "ety", 0, 0, tiled=True).reshape(chips, 1, own_rows, -1)
    z_fwd = jnp.dot(act_fwd, w_down, preferred_element_type=jnp.float32).astype(jnp.bfloat16)
    z_fwd = z_fwd.reshape(chips, 2, own_rows, width)
    mine_z = jnp.where(core == 0, z_fwd[:, 0], z_fwd[:, 1])
    give_z = jnp.where(core == 0, z_fwd[:, 1], z_fwd[:, 0])
    given = lax.ppermute(give_z, "etc", [(0, 1), (1, 0)])
    pair_z = (mine_z.astype(jnp.float32) + given.astype(jnp.float32)).astype(jnp.bfloat16)
    pair_z, same_core = lax.optimization_barrier((pair_z, same_core))
    got = lax.all_to_all(pair_z.reshape(chips * own_rows, width), "ety", 0, 0, tiled=True)

    other_core = lax.ppermute(same_core, "etc", [(0, 1), (1, 0)])
    full = jnp.where(
        core == 0,
        jnp.concatenate([same_core, other_core], axis=1),
        jnp.concatenate([other_core, same_core], axis=1),
    ).reshape(groups * own_rows, -1)
    full_g = full[:, :width]
    full_b = full[:, width : width + experts]

    _, _, _, coef_b = routing(full_b, ids_bwd, experts)
    back_up = lax.dot_general(
        full_g, w_down, (((1,), (1,)), ((), ())), preferred_element_type=jnp.float32
    )
    dact = (coef_b[:, None] * back_up).astype(jnp.bfloat16)
    dprob_part = jnp.sum(act_bwd.astype(jnp.float32) * back_up, axis=1)
    halves = dprob_part.reshape(chips, 2, own_rows)
    keep = jnp.where(core == 0, halves[:, 0], halves[:, 1])
    give = jnp.where(core == 0, halves[:, 1], halves[:, 0])
    pair_d = keep + lax.ppermute(give, "etc", [(0, 1), (1, 0)])
    pair_d, got = lax.optimization_barrier((pair_d, got))
    dprob_got = lax.all_to_all(pair_d, "ety", 0, 0, tiled=True)
    dprob_mine = jnp.sum(dprob_got, axis=0)
    z_sum = jnp.sum(got.reshape(chips, own_rows, width).astype(jnp.float32), axis=0)

    ids_f_own = lax.dynamic_slice_in_dim(ids_fwd, first_row, own_rows, 0)
    _, _, _, coef_f = routing(logit_f, ids_f_own, experts)
    layer_out = (wide_f + coef_f[:, None] * z_sum).astype(jnp.bfloat16)

    ids_b_own = lax.dynamic_slice_in_dim(ids_bwd, first_row, own_rows, 0)
    route_mine, onehot_mine, sigma_mine, _ = routing(logit_b, ids_b_own, experts)
    router_wide = w_router.astype(jnp.float32)
    spread = router_wide[:, 0][None, :] - jnp.dot(
        onehot_mine, router_wide.T, precision=lax.Precision.HIGHEST
    )
    scaled_rows = spread * gain.astype(jnp.float32)
    normalized_input = backward_wide_rows * backward_inverse_norm
    along = (route_mine * sigma_mine * (1.0 - sigma_mine))[:, None] * backward_inverse_norm * (
        scaled_rows
        - normalized_input * jnp.mean(scaled_rows * normalized_input, axis=-1, keepdims=True)
    )
    norm_input_gradient = dprob_mine[:, None] * along
    input_grad = (grad_out.astype(jnp.float32) + norm_input_gradient).astype(jnp.bfloat16)
    fwd_in = from_behind(layer_out[None], "section", 1)
    incoming_gradient = from_behind(input_grad[None], "section", -1)
    return (fwd_in, incoming_gradient, dact[None])


def solution(mesh):
    sections, ets = mesh.devices.shape
    mesh = jax.sharding.Mesh(mesh.devices.reshape(sections, ets // 2, 2), ("section", "ety", "etc"))
    et = ("ety", "etc")
    placed = (
        P("section", et, None),
        P("section", None, et),
        P("section", None, None),
        P("section", et, None),
        P("section", None, et),
        P("section", None, None),
        P("section", et, None),
        P("section", None),
        P("section", None, None),
        P("section", et, None),
    )
    return jax.shard_map(
        layer,
        mesh=mesh,
        in_specs=placed,
        out_specs=(P("section", et, None), P("section", et, None), P("section", None, et)),
        check_vma=False,
    )
```

```python
import jax
import jax.numpy as jnp
from jax import lax
from jax.sharding import PartitionSpec as P


def from_behind(value, axis, steps):
    count = lax.axis_size(axis)
    first, last = (max(0, -steps), min(count, count - steps))
    return lax.ppermute(value, axis, [(source, source + steps) for source in range(first, last)])


def norm_logits(inputs, gain, w_router):
    wide = inputs.astype(jnp.float32)
    inverse = lax.rsqrt(jnp.mean(wide * wide, axis=-1, keepdims=True) + 1e-05)
    normed = (wide * inverse * gain.astype(jnp.float32)).astype(jnp.bfloat16)
    logits = jnp.dot(normed, w_router, preferred_element_type=jnp.float32).astype(jnp.bfloat16)
    return (wide, inverse, logits)


def routing(logits, chosen, experts):
    route = jnp.sum((chosen == 0).astype(jnp.float32), axis=1)
    partner = jnp.minimum(jnp.sum(chosen, axis=1), experts - 1)
    labels = jnp.arange(experts, dtype=jnp.int32)
    onehot = (partner[:, None] == labels[None, :]).astype(jnp.float32)
    wide_logits = logits.astype(jnp.float32)
    sigma = jax.nn.sigmoid(wide_logits[:, 0] - jnp.sum(wide_logits * onehot, axis=1))
    return (route, onehot, sigma, route * sigma)


def layer(x_fwd, act_fwd, ids_fwd, x_bwd, act_bwd, ids_bwd, grad_out, gain, w_router, w_down):
    x_fwd, act_fwd, ids_fwd, x_bwd, act_bwd = (x_fwd[0], act_fwd[0], ids_fwd[0], x_bwd[0], act_bwd[0])
    ids_bwd, grad_out, gain, w_router, w_down = (ids_bwd[0], grad_out[0], gain[0], w_router[0], w_down[0])
    experts = w_router.shape[1]
    width = x_fwd.shape[1]
    own_rows = x_fwd.shape[0]
    groups = lax.axis_size("ety") * lax.axis_size("etc")
    first_row = (lax.axis_index("ety") * lax.axis_size("etc") + lax.axis_index("etc")) * own_rows
    pad = 128

    wide_f, _, logit_f = norm_logits(x_fwd, gain, w_router)
    backward_wide_rows, backward_inverse_norm, logit_b = norm_logits(x_bwd, gain, w_router)

    packed = jnp.concatenate(
        [grad_out, jnp.pad(logit_b, ((0, 0), (0, pad - experts)))], axis=1
    )
    chips = lax.axis_size("ety")
    core = lax.axis_index("etc")
    tiled = jnp.broadcast_to(packed[None], (chips,) + packed.shape).reshape(chips * own_rows, -1)
    same_core = lax.all_to_all(tiled, "ety", 0, 0, tiled=True).reshape(chips, 1, own_rows, -1)
    z_fwd = jnp.dot(act_fwd, w_down, preferred_element_type=jnp.float32).astype(jnp.bfloat16)
    z_fwd = z_fwd.reshape(chips, 2, own_rows, width)
    mine_z = jnp.where(core == 0, z_fwd[:, 0], z_fwd[:, 1])
    give_z = jnp.where(core == 0, z_fwd[:, 1], z_fwd[:, 0])
    given = lax.ppermute(give_z, "etc", [(0, 1), (1, 0)])
    pair_z = (mine_z.astype(jnp.float32) + given.astype(jnp.float32)).astype(jnp.bfloat16)
    pair_z, same_core = lax.optimization_barrier((pair_z, same_core))
    got = lax.all_to_all(pair_z.reshape(chips * own_rows, width), "ety", 0, 0, tiled=True)

    other_core = lax.ppermute(same_core, "etc", [(0, 1), (1, 0)])
    full = jnp.where(
        core == 0,
        jnp.concatenate([same_core, other_core], axis=1),
        jnp.concatenate([other_core, same_core], axis=1),
    ).reshape(groups * own_rows, -1)
    full_g = full[:, :width]
    full_b = full[:, width : width + experts]

    _, _, _, coef_b = routing(full_b, ids_bwd, experts)
    back_up = lax.dot_general(
        full_g, w_down, (((1,), (1,)), ((), ())), preferred_element_type=jnp.float32
    )
    dact = (coef_b[:, None] * back_up).astype(jnp.bfloat16)
    dprob_part = jnp.sum(act_bwd.astype(jnp.float32) * back_up, axis=1)
    halves = dprob_part.reshape(chips, 2, own_rows)
    keep = jnp.where(core == 0, halves[:, 0], halves[:, 1])
    give = jnp.where(core == 0, halves[:, 1], halves[:, 0])
    pair_d = keep + lax.ppermute(give, "etc", [(0, 1), (1, 0)])
    pair_d, got = lax.optimization_barrier((pair_d, got))
    chip = lax.axis_index("ety")
    span = chips // 2
    while span >= 1:
        bit = (chip // span) % 2
        split = pair_d.reshape(2, -1, own_rows)
        keep = jnp.where(bit == 0, split[0], split[1])
        give = jnp.where(bit == 0, split[1], split[0])
        pair_d = keep + lax.ppermute(give, "ety", [(i, i ^ span) for i in range(chips)])
        span //= 2
    dprob_mine = pair_d.reshape(own_rows)
    z_sum = jnp.sum(got.reshape(chips, own_rows, width).astype(jnp.float32), axis=0)

    ids_f_own = lax.dynamic_slice_in_dim(ids_fwd, first_row, own_rows, 0)
    _, _, _, coef_f = routing(logit_f, ids_f_own, experts)
    layer_out = (wide_f + coef_f[:, None] * z_sum).astype(jnp.bfloat16)

    ids_b_own = lax.dynamic_slice_in_dim(ids_bwd, first_row, own_rows, 0)
    route_mine, onehot_mine, sigma_mine, _ = routing(logit_b, ids_b_own, experts)
    router_wide = w_router.astype(jnp.float32)
    spread = router_wide[:, 0][None, :] - jnp.dot(
        onehot_mine, router_wide.T, precision=lax.Precision.HIGHEST
    )
    scaled_rows = spread * gain.astype(jnp.float32)
    normalized_input = backward_wide_rows * backward_inverse_norm
    along = (route_mine * sigma_mine * (1.0 - sigma_mine))[:, None] * backward_inverse_norm * (
        scaled_rows
        - normalized_input * jnp.mean(scaled_rows * normalized_input, axis=-1, keepdims=True)
    )
    norm_input_gradient = dprob_mine[:, None] * along
    input_grad = (grad_out.astype(jnp.float32) + norm_input_gradient).astype(jnp.bfloat16)
    fwd_in = from_behind(layer_out[None], "section", 1)
    incoming_gradient = from_behind(input_grad[None], "section", -1)
    return (fwd_in, incoming_gradient, dact[None])


def solution(mesh):
    sections, ets = mesh.devices.shape
    mesh = jax.sharding.Mesh(mesh.devices.reshape(sections, ets // 2, 2), ("section", "ety", "etc"))
    et = ("ety", "etc")
    placed = (
        P("section", et, None),
        P("section", None, et),
        P("section", None, None),
        P("section", et, None),
        P("section", None, et),
        P("section", None, None),
        P("section", et, None),
        P("section", None),
        P("section", None, None),
        P("section", et, None),
    )
    return jax.shard_map(
        layer,
        mesh=mesh,
        in_specs=placed,
        out_specs=(P("section", et, None), P("section", et, None), P("section", None, et)),
        check_vma=False,
    )
```
